512 devices in a mesh: lat: 64 (over y, x, core), row: 8 (over z).
Axes of the slice: x: 4, y: 8, z: 8, core: 2. Of those that a mesh axis runs over, the one named last changes fastest.
Arguments:
- activations: float32 [12288, 8192], P('lat', 'row'), may hold values from -15 to 15
- center_bias: float32 [8192], P('row'), may hold values from -3 to 3
- encoder_weight: bfloat16 [8192, 16384], P('row', 'lat'), may hold values from -0.0625 to 0.0625
- encoder_bias: float32 [16384], P('lat'), may hold values from -3 to 3
- decoder_weight: bfloat16 [16384, 8192], P('lat', 'row'), may hold values from -1 to 1
- row_blocks: int32 [12288, 4], P('lat'), may hold values from 0 to 127, all different within a row; in each aligned block of 192 rows (0 to 191, 192 to 383, ...) at most 12 rows name the same one
- pick_offsets: int32 [12288, 4, 8], P('lat'), may hold values from 0 to 127
Outputs:
- encoder_grad: bfloat16 [8192, 16384], P('row', 'lat')
- decoder_grad: bfloat16 [16384, 8192], P('lat', 'row')
- bias_grad: float32 [16384], P('lat')
- row_loss: float32 [12288], P('lat')
The draws below stay inside these ranges and needn't reach their ends.
Inputs may be any that keep to these rules, and one draw needn't show every extreme that they name: `row_blocks`: the 4 blocks of a row differ. Within each group of 192 rows (the rows of one lat index), at most 12 rows name the same block, and in some groups one block is named by exactly 12 rows.
All inputs are finite; a program needn't handle non-finite values.
Results may differ from the reference program's by a relative error of at most 0.006.
Values may be sent and summed in bfloat16 or wider, within the bound.
No kernel may reach another device: no remote copies, remote signals or barrier semaphores. Data moves between devices by JAX's collectives and lax.ppermute only.
A program may use at most 64 MiB of HBM per device.

```python
import math
import jax
import jax.numpy as jnp
import numpy as np
from jax import lax

D = 8192
BLK = 128
BLK_DEV = 2
RG = 192
KB = 4
PER = 8
TOPK = 32
CAPR = 12
NBLK = 128
LATENTS = 16384
ROWS = 12288
N_LAT = 64


def draw_activations(key, part):
    key_main = jax.random.fold_in(key, 11)
    columns = jnp.arange(D, dtype=jnp.float32) / (D - 1)
    rising = jnp.exp(jnp.log(3.0) * columns)
    values = jax.random.truncated_normal(key_main, -4.0, 4.0, (ROWS, D), jnp.float32) * (0.6 * rising)[None, :]
    return values


def place_ends(result, own_key, smallest, high):
    longest = result.shape.index(max(result.shape))
    spots = []
    for shift in (0, 1):
        where = [jax.random.randint(jax.random.fold_in(own_key, axis), (), 0, length) for axis, length in enumerate(result.shape)]
        where[longest] = (where[longest] + shift) % result.shape[longest]
        spots.append(tuple(where))
    return result.at[spots[0]].set(smallest).at[spots[1]].set(high)


def level_of(own_key, shape, pieces, smallest, top_value):
    loudness, own = 1.0, jax.random.fold_in(own_key, 6)
    for axis_at, parts in pieces:
        steps = jnp.exp(jax.random.uniform(jax.random.fold_in(own, axis_at), (parts,), jnp.float32, smallest / len(pieces), top_value / len(pieces)))
        loudness = loudness * jnp.repeat(steps, shape[axis_at] // parts).reshape([-1 if axis == axis_at else 1 for axis in range(len(shape))])
    return loudness


def shared_out(own_key, own, number, rows, amount, top, limit, slope):
    sequence = jax.random.permutation(own_key, amount)
    crowded, ordinary = portions_of(amount, rows * top, limit, slope, True), portions_of(amount, rows * top, limit, slope, False)
    places = jnp.arange(amount)

    def named(tallies, turn):
        used = int((tallies > 0).sum())
        fixed = max(1, used // 4)
        passed = fixed + (places - fixed + turn * (used - fixed)) % max(1, amount - fixed)
        return jnp.zeros((amount,), jnp.int32).at[sequence[jnp.where(places < fixed, places, passed)]].set(jnp.asarray(tallies, jnp.int32))

    tallies = jnp.where(number % 4 == 0, named(crowded, number // 4), named(ordinary, number - number // 4 - 1))
    mixed = jax.random.permutation(jax.random.fold_in(own, 3), amount)
    donor, sink = mixed[0:amount // 2 * 2:2], mixed[1:amount // 2 * 2:2]
    slack = jnp.minimum(tallies[donor] - 1, limit - tallies[sink]) // 2
    slack = jnp.where((donor == sequence[0]) | (sink == sequence[0]) | (tallies[sink] == 0), 0, jnp.maximum(slack, 0))
    passed = jax.random.randint(jax.random.fold_in(own, 4), (amount // 2,), 0, 1 << 20) % (slack + 1)
    tallies = tallies.at[donor].add(-passed).at[sink].add(passed)
    labels = jnp.searchsorted(jnp.cumsum(tallies), jnp.arange(rows * top), side="right").astype(jnp.int32)
    listing = labels.reshape(top, rows).T
    listing = listing[jax.random.permutation(jax.random.fold_in(own, 1), rows)]
    turn = jax.random.randint(jax.random.fold_in(own, 2), (rows, 1), 0, top)
    return jnp.take_along_axis(listing, (jnp.arange(top)[None, :] + turn) % top, axis=1)


def portions_of(number_of, total, most, slope, full):
    loads = [(1 << 20) // math.isqrt(grade ** slope) + 1 for grade in range(1, number_of + 1)]
    largest = most if full else min(most, max(-(-total // number_of), total * loads[0] // sum(loads)))
    least = 1 if total - largest >= number_of - 1 else 0
    holding, surplus = [largest] + [least] * (number_of - 1), total - largest - least * (number_of - 1)
    while surplus > 0:
        free = [i for i in range(1, number_of) if holding[i] < largest] or [i for i in range(1, number_of) if holding[i] < most]
        mass, budget = sum([loads[i] for i in free]), surplus
        for i in free:
            extra = min(most - holding[i], max(1, budget * loads[i] // mass), surplus)
            holding[i] = holding[i] + extra
            surplus = surplus - extra
    return np.array(holding)


def bell_draw(stream_key, dims, spread, limit, cuts=(), kind=jnp.bfloat16):
    level = level_of(stream_key, dims, cuts, -0.22, 0.18) if cuts else 1.0
    drawn = jax.random.normal(stream_key, dims, jnp.float32) * spread * level
    return jnp.minimum(jnp.maximum(drawn, -limit), limit).astype(kind)


def setup_inputs(seed: int = 0) -> dict:
    arg_keys = jax.random.split(jax.random.key(seed), 8)
    activations = draw_activations(jax.random.fold_in(arg_keys[7], 71), 0)
    center_bias = bell_draw(arg_keys[1], (D,), 0.5, 3.0, ((0, 8),), jnp.float32)
    encoder_weight = bell_draw(arg_keys[2], (D, LATENTS), D ** -0.5, 0.0625, ((0, 8), (1, 64)))
    encoder_bias = bell_draw(arg_keys[3], (LATENTS,), 0.5, 3.0, ((0, 64),), jnp.float32)
    decoder_weight = bell_draw(arg_keys[4], (LATENTS, D), TOPK ** -0.5, 1.0, ((0, 64), (1, 8)))
    row_blocks_keys = jax.random.split(jax.random.fold_in(arg_keys[5], 1), ROWS // RG)
    row_blocks_turns = jax.random.permutation(jax.random.fold_in(arg_keys[5], 3), ROWS // RG)
    row_blocks = jax.vmap(lambda own, number: shared_out(jax.random.fold_in(arg_keys[5], 2), own, number, RG, NBLK, KB, CAPR, 2))(row_blocks_keys, row_blocks_turns).reshape((ROWS, KB))
    pick_offsets = place_ends(jax.random.randint(arg_keys[6], (ROWS, KB, PER), 0, BLK), jax.random.fold_in(arg_keys[6], 1), 0, BLK - 1).astype(jnp.int32)
    return dict(activations=activations, center_bias=center_bias, encoder_weight=encoder_weight, encoder_bias=encoder_bias, decoder_weight=decoder_weight, row_blocks=row_blocks, pick_offsets=pick_offsets)


def reference(activations, center_bias, encoder_weight, encoder_bias, decoder_weight, row_blocks, pick_offsets):
    total_blocks = BLK_DEV * N_LAT
    pair_count = ROWS * KB
    grouped = row_blocks.reshape(N_LAT, RG * KB)
    onehot = (grouped[:, :, None] == jnp.arange(total_blocks, dtype=jnp.int32)[None, None, :]).astype(jnp.int32)
    before = jnp.cumsum(onehot, axis=1) - onehot
    ranking = jnp.sum(before * onehot, axis=2).astype(jnp.int32)
    pair_ids = jnp.arange(pair_count, dtype=jnp.int32).reshape(N_LAT, RG * KB)
    group_ids = jnp.broadcast_to(jnp.arange(N_LAT, dtype=jnp.int32)[:, None], (N_LAT, RG * KB))
    pair_table = jnp.full((total_blocks, N_LAT, CAPR), pair_count, jnp.int32)
    pair_table = pair_table.at[grouped, group_ids, ranking].set(pair_ids)
    pair_table = pair_table.reshape(total_blocks, N_LAT * CAPR)

    centered = (activations - center_bias[None, :]).astype(jnp.bfloat16)
    centered_pad = jnp.concatenate([centered, jnp.zeros((1, D), centered.dtype)], axis=0)
    offsets_pad = jnp.concatenate([pick_offsets.reshape(pair_count, PER), jnp.full((1, PER), -1, jnp.int32)], axis=0)
    latent_ids = jnp.arange(BLK, dtype=jnp.int32)

    def block_inputs(block):
        slot_pairs = pair_table[block]
        slot_rows = (slot_pairs // KB).astype(jnp.int32)
        rows_in = centered_pad[slot_rows]
        chosen = jnp.any(offsets_pad[slot_pairs][:, :, None] == latent_ids[None, None, :], axis=1).astype(jnp.float32)
        first_col = (block * BLK).astype(jnp.int32)
        enc_block = lax.dynamic_slice_in_dim(encoder_weight, first_col, BLK, 1)
        dec_block = lax.dynamic_slice_in_dim(decoder_weight, first_col, BLK, 0)
        return slot_rows, rows_in, chosen, enc_block, dec_block, first_col

    def forward(rebuilt, block):
        slot_rows, rows_in, chosen, enc_block, dec_block, first_col = block_inputs(block)
        pre = jnp.dot(rows_in, enc_block, preferred_element_type=jnp.float32)
        pre = pre + lax.dynamic_slice_in_dim(encoder_bias, first_col, BLK, 0)[None, :]
        latent = (pre * chosen).astype(jnp.bfloat16)
        decoded = jnp.dot(latent, dec_block, preferred_element_type=jnp.float32).astype(jnp.bfloat16)
        decoded = lax.optimization_barrier(decoded).astype(jnp.float32)
        return rebuilt.at[slot_rows].add(decoded), latent

    blocks_seq = jnp.arange(total_blocks, dtype=jnp.int32)
    rebuilt, latents = lax.scan(forward, jnp.zeros((ROWS + 1, D), jnp.float32), blocks_seq)
    recon_error = center_bias[None, :] + rebuilt[:ROWS] - activations
    row_loss = jnp.sum(recon_error * recon_error, axis=1) / D
    error_b = recon_error.astype(jnp.bfloat16)
    error_pad = jnp.concatenate([error_b, jnp.zeros((1, D), error_b.dtype)], axis=0)

    def backward(block_and_latent):
        block, latent = block_and_latent
        slot_rows, rows_in, chosen, enc_block, dec_block, first_col = block_inputs(block)
        error_rows = error_pad[slot_rows]
        dlatent = jnp.dot(error_rows, dec_block.T, preferred_element_type=jnp.float32)
        grad_pre = (dlatent * chosen).astype(jnp.bfloat16)
        dec_grad = jnp.dot(latent.T, error_rows, preferred_element_type=jnp.float32).astype(jnp.bfloat16)
        enc_grad = jnp.dot(rows_in.T, grad_pre, preferred_element_type=jnp.float32).astype(jnp.bfloat16)
        bias_grad = jnp.sum(grad_pre.astype(jnp.float32), axis=0)
        return dec_grad, enc_grad, bias_grad

    dec_all, enc_all, bias_all = lax.map(backward, (blocks_seq, latents))
    encoder_grad = jnp.transpose(enc_all, (1, 0, 2)).reshape(D, total_blocks * BLK)
    decoder_grad = dec_all.reshape(total_blocks * BLK, D)
    bias_grad = bias_all.reshape(total_blocks * BLK)
    return encoder_grad, decoder_grad, bias_grad, row_loss
```

```python
import jax
import jax.numpy as jnp
from jax import lax
from jax.sharding import PartitionSpec as P

D = 8192
BLK = 128
KB = 4
PER = 8


def slot_targets(row_blocks, total_blocks, capacity):
    pair_blocks = row_blocks.reshape(-1)
    onehot = (pair_blocks[:, None] == jnp.arange(total_blocks, dtype=jnp.int32)[None, :]).astype(
        jnp.int32
    )
    before = jnp.cumsum(onehot, axis=0) - onehot
    ranking = jnp.sum(before * onehot, axis=1)
    return pair_blocks * capacity + ranking


def pick_columns(values, offsets):
    lanes = jnp.arange(BLK, dtype=jnp.int32)
    hit = offsets[:, :, None] == lanes[None, None, :]
    return jnp.sum(jnp.where(hit, values[:, None, :], 0.0), axis=2)


def spread_columns(picked, offsets):
    lanes = jnp.arange(BLK, dtype=jnp.int32)[None, :]
    out = jnp.zeros((picked.shape[0], BLK), picked.dtype)
    for j in range(PER):
        out = jnp.where(offsets[:, j : j + 1] == lanes, picked[:, j : j + 1], out)
    return out


def per_device(
    activations, center_bias, encoder_weight, encoder_bias, decoder_weight, row_blocks, pick_offsets
):
    group_rows, feature_width = activations.shape
    owners = lax.axis_size("lat")
    owned_blocks = encoder_bias.shape[0] // BLK
    total_blocks = owned_blocks * owners
    capacity = 2 * group_rows * KB // total_blocks
    slot_count = total_blocks * capacity
    per_owner = owned_blocks * capacity
    target = slot_targets(row_blocks, total_blocks, capacity)
    slots = jnp.arange(slot_count, dtype=jnp.int32)

    pair_hot = target[None, :] == slots[:, None]
    row_hot = jnp.any(pair_hot.reshape(slot_count, group_rows, KB), axis=2).astype(jnp.bfloat16)
    pair_hot = pair_hot.astype(jnp.bfloat16)

    centered = (activations - center_bias[None, :]).astype(jnp.bfloat16)
    outgoing = jnp.dot(row_hot, centered, preferred_element_type=jnp.float32).astype(jnp.bfloat16)
    offs_plus = (pick_offsets.reshape(-1, PER) + 1).astype(jnp.bfloat16)
    out_offs = jnp.dot(pair_hot, offs_plus, preferred_element_type=jnp.float32).astype(jnp.int32)

    got_offs = lax.all_to_all(
        out_offs.reshape(owners, per_owner, PER), "lat", split_axis=0, concat_axis=0, tiled=True
    )
    got_rows = lax.all_to_all(
        outgoing.reshape(owners, per_owner, feature_width),
        "lat",
        split_axis=0,
        concat_axis=0,
        tiled=True,
    )
    got_rows = got_rows.reshape(slot_count, feature_width)
    offs = got_offs.reshape(slot_count, PER) - 1

    slot_block = (slots // capacity) % owned_blocks
    col_block = jnp.arange(owned_blocks * BLK, dtype=jnp.int32) // BLK
    own_col = slot_block[:, None] == col_block[None, :]

    def own_half(full):
        parts = full.reshape(slot_count, owned_blocks, BLK)
        sel = slot_block[:, None, None] == jnp.arange(owned_blocks, dtype=jnp.int32)[None, :, None]
        return jnp.sum(jnp.where(sel, parts, 0.0), axis=1)

    def widen(narrow):
        tiled = jnp.tile(narrow, (1, owned_blocks))
        return jnp.where(own_col, tiled, jnp.zeros_like(tiled))

    partial_full = jnp.dot(got_rows, encoder_weight, preferred_element_type=jnp.float32)
    partial = pick_columns(own_half(partial_full), offs)
    summed = lax.psum(partial, "row")
    bias_rows = own_half(jnp.broadcast_to(encoder_bias[None, :], (slot_count, owned_blocks * BLK)))
    pre_picked = summed + pick_columns(bias_rows, offs)
    latent = spread_columns(pre_picked, offs).astype(jnp.bfloat16)
    latent_wide = widen(latent)
    decoded = jnp.dot(latent_wide, decoder_weight, preferred_element_type=jnp.float32).astype(
        jnp.bfloat16
    )
    returned = lax.all_to_all(
        decoded.reshape(owners, per_owner, feature_width),
        "lat",
        split_axis=0,
        concat_axis=0,
        tiled=True,
    ).reshape(slot_count, feature_width)
    rebuilt = lax.dot_general(
        row_hot, returned, (((0,), (0,)), ((), ())), preferred_element_type=jnp.float32
    )
    recon_error = (center_bias[None, :] + rebuilt) - activations
    loss_part = jnp.sum(recon_error * recon_error, axis=1)
    error_b = recon_error.astype(jnp.bfloat16)
    out_error = jnp.dot(row_hot, error_b, preferred_element_type=jnp.float32).astype(jnp.bfloat16)
    got_error = lax.all_to_all(
        out_error.reshape(owners, per_owner, feature_width),
        "lat",
        split_axis=0,
        concat_axis=0,
        tiled=True,
    ).reshape(slot_count, feature_width)
    decoder_grad = lax.dot_general(
        latent_wide, got_error, (((0,), (0,)), ((), ())), preferred_element_type=jnp.float32
    ).astype(jnp.bfloat16)
    dlatent_full = lax.dot_general(
        got_error, decoder_weight, (((1,), (1,)), ((), ())), preferred_element_type=jnp.float32
    )
    dlatent_part = pick_columns(own_half(dlatent_full), offs)
    dlatent, loss_total = lax.psum((dlatent_part, loss_part), "row")
    grad_pre = spread_columns(dlatent, offs).astype(jnp.bfloat16)
    grad_wide = widen(grad_pre)
    encoder_grad = lax.dot_general(
        got_rows, grad_wide, (((0,), (0,)), ((), ())), preferred_element_type=jnp.float32
    ).astype(jnp.bfloat16)
    bias_grad = jnp.sum(grad_wide.astype(jnp.float32), axis=0)
    row_loss = loss_total / D
    return (encoder_grad, decoder_grad, bias_grad, row_loss)


def solution(mesh):
    return jax.shard_map(
        per_device,
        mesh=mesh,
        in_specs=(
            P("lat", "row"),
            P("row"),
            P("row", "lat"),
            P("lat"),
            P("lat", "row"),
            P("lat", None),
            P("lat", None, None),
        ),
        out_specs=(P("row", "lat"), P("lat", "row"), P("lat"), P("lat")),
        check_vma=False,
    )
```

```python
import jax
import jax.numpy as jnp
from jax import lax
from jax.sharding import PartitionSpec as P

D = 8192
BLK = 128
KB = 4
PER = 8


def slot_targets(row_blocks, total_blocks, capacity):
    pair_blocks = row_blocks.reshape(-1)
    onehot = (pair_blocks[:, None] == jnp.arange(total_blocks, dtype=jnp.int32)[None, :]).astype(
        jnp.int32
    )
    before = jnp.cumsum(onehot, axis=0) - onehot
    ranking = jnp.sum(before * onehot, axis=1)
    return pair_blocks * capacity + ranking


def pick_rows(values_t, offsets_t):
    lanes = jnp.arange(BLK, dtype=jnp.int32)
    hit = offsets_t[:, None, :] == lanes[None, :, None]
    return jnp.sum(jnp.where(hit, values_t[None, :, :], 0.0), axis=1)


def spread_rows(picked_t, offsets_t):
    lanes = jnp.arange(BLK, dtype=jnp.int32)[:, None]
    out = jnp.zeros((BLK, picked_t.shape[1]), picked_t.dtype)
    for j in range(PER):
        out = jnp.where(offsets_t[j : j + 1, :] == lanes, picked_t[j : j + 1, :], out)
    return out


def per_device(
    activations, center_bias, encoder_weight, encoder_bias, decoder_weight, row_blocks, pick_offsets
):
    group_rows, feature_width = activations.shape
    owners = lax.axis_size("lat")
    owned_blocks = encoder_bias.shape[0] // BLK
    owned_cols = owned_blocks * BLK
    total_blocks = owned_blocks * owners
    capacity = 2 * group_rows * KB // total_blocks
    slot_count = total_blocks * capacity
    per_owner = owned_blocks * capacity
    target = slot_targets(row_blocks, total_blocks, capacity)
    slots = jnp.arange(slot_count, dtype=jnp.int32)

    pair_hot = target[None, :] == slots[:, None]
    row_hot = jnp.any(pair_hot.reshape(slot_count, group_rows, KB), axis=2).astype(jnp.bfloat16)
    pair_hot = pair_hot.astype(jnp.bfloat16)

    centered = (activations - center_bias[None, :]).astype(jnp.bfloat16)
    outgoing = jnp.dot(row_hot, centered, preferred_element_type=jnp.float32).astype(jnp.bfloat16)
    offs_plus = (pick_offsets.reshape(-1, PER) + 1).astype(jnp.bfloat16)
    out_offs_t = lax.dot_general(
        offs_plus, pair_hot, (((0,), (1,)), ((), ())), preferred_element_type=jnp.float32
    ).astype(jnp.int32)
    out_offs = out_offs_t.reshape(PER, owners, per_owner).transpose(1, 0, 2)

    got_offs = lax.all_to_all(out_offs, "lat", split_axis=0, concat_axis=0, tiled=True)
    got_rows = lax.all_to_all(
        outgoing.reshape(owners, per_owner, feature_width),
        "lat",
        split_axis=0,
        concat_axis=0,
        tiled=True,
    )
    got_rows = got_rows.reshape(slot_count, feature_width)
    offs_t = got_offs.transpose(1, 0, 2).reshape(PER, slot_count) - 1

    slot_block = (slots // capacity) % owned_blocks
    col_block = jnp.arange(owned_cols, dtype=jnp.int32) // BLK
    own_col = col_block[:, None] == slot_block[None, :]

    def own_half(full_t):
        parts = full_t.reshape(owned_blocks, BLK, slot_count)
        sel = jnp.arange(owned_blocks, dtype=jnp.int32)[:, None, None] == slot_block[None, None, :]
        return jnp.sum(jnp.where(sel, parts, 0.0), axis=0)

    def widen(narrow_t):
        tiled = jnp.tile(narrow_t, (owned_blocks, 1))
        return jnp.where(own_col, tiled, jnp.zeros_like(tiled))

    partial_t = lax.dot_general(
        encoder_weight, got_rows, (((0,), (1,)), ((), ())), preferred_element_type=jnp.float32
    )
    partial = pick_rows(own_half(partial_t), offs_t)
    summed = lax.psum(partial, "row")
    bias_t = own_half(jnp.broadcast_to(encoder_bias[:, None], (owned_cols, slot_count)))
    pre_picked = summed + pick_rows(bias_t, offs_t)
    latent_t = spread_rows(pre_picked, offs_t).astype(jnp.bfloat16)
    latent_wide_t = widen(latent_t)
    decoded = lax.dot_general(
        latent_wide_t, decoder_weight, (((0,), (0,)), ((), ())), preferred_element_type=jnp.float32
    ).astype(jnp.bfloat16)
    returned = lax.all_to_all(
        decoded.reshape(owners, per_owner, feature_width),
        "lat",
        split_axis=0,
        concat_axis=0,
        tiled=True,
    ).reshape(slot_count, feature_width)
    rebuilt = lax.dot_general(
        row_hot, returned, (((0,), (0,)), ((), ())), preferred_element_type=jnp.float32
    )
    recon_error = (center_bias[None, :] + rebuilt) - activations
    loss_part = jnp.sum(recon_error * recon_error, axis=1)
    error_b = recon_error.astype(jnp.bfloat16)
    out_error = jnp.dot(row_hot, error_b, preferred_element_type=jnp.float32).astype(jnp.bfloat16)
    got_error = lax.all_to_all(
        out_error.reshape(owners, per_owner, feature_width),
        "lat",
        split_axis=0,
        concat_axis=0,
        tiled=True,
    ).reshape(slot_count, feature_width)
    decoder_grad = lax.dot_general(
        latent_wide_t, got_error, (((1,), (0,)), ((), ())), preferred_element_type=jnp.float32
    ).astype(jnp.bfloat16)
    dlatent_t = lax.dot_general(
        decoder_weight, got_error, (((1,), (1,)), ((), ())), preferred_element_type=jnp.float32
    )
    dlatent_part = pick_rows(own_half(dlatent_t), offs_t)
    dlatent, loss_total = lax.psum((dlatent_part, loss_part), "row")
    grad_t = spread_rows(dlatent, offs_t).astype(jnp.bfloat16)
    grad_wide_t = widen(grad_t)
    encoder_grad = lax.dot_general(
        got_rows, grad_wide_t, (((0,), (1,)), ((), ())), preferred_element_type=jnp.float32
    ).astype(jnp.bfloat16)
    bias_grad = jnp.sum(grad_wide_t.astype(jnp.float32), axis=1)
    row_loss = loss_total / D
    return (encoder_grad, decoder_grad, bias_grad, row_loss)


def solution(mesh):
    return jax.shard_map(
        per_device,
        mesh=mesh,
        in_specs=(
            P("lat", "row"),
            P("row"),
            P("row", "lat"),
            P("lat"),
            P("lat", "row"),
            P("lat", None),
            P("lat", None, None),
        ),
        out_specs=(P("row", "lat"), P("lat", "row"), P("lat"), P("lat")),
        check_vma=False,
    )
```

```python
import jax
import jax.numpy as jnp
from jax import lax
from jax.sharding import PartitionSpec as P

D = 8192
BLK = 128
KB = 4
PER = 8


def slot_targets(row_blocks, total_blocks, capacity):
    pair_blocks = row_blocks.reshape(-1)
    onehot = (pair_blocks[:, None] == jnp.arange(total_blocks, dtype=jnp.int32)[None, :]).astype(
        jnp.int32
    )
    before = jnp.cumsum(onehot, axis=0) - onehot
    ranking = jnp.sum(before * onehot, axis=1)
    return pair_blocks * capacity + ranking


def pick_rows(values_t, offsets_t):
    lanes = jnp.arange(BLK, dtype=jnp.int32)
    hit = offsets_t[:, None, :] == lanes[None, :, None]
    return jnp.sum(jnp.where(hit, values_t[None, :, :], 0.0), axis=1)


def spread_rows(picked_t, offsets_t):
    lanes = jnp.arange(BLK, dtype=jnp.int32)[:, None]
    out = jnp.zeros((BLK, picked_t.shape[1]), picked_t.dtype)
    for j in range(PER):
        out = jnp.where(offsets_t[j : j + 1, :] == lanes, picked_t[j : j + 1, :], out)
    return out


def butterfly_sum(x, axis):
    size = lax.axis_size(axis)
    step = 1
    while step < size:
        other = lax.ppermute(x, axis, perm=[(i, i ^ step) for i in range(size)])
        x = x + other
        step *= 2
    return x


def per_device(
    activations, center_bias, encoder_weight, encoder_bias, decoder_weight, row_blocks, pick_offsets
):
    group_rows, feature_width = activations.shape
    owners = lax.axis_size("lat")
    owned_blocks = encoder_bias.shape[0] // BLK
    owned_cols = owned_blocks * BLK
    total_blocks = owned_blocks * owners
    capacity = 2 * group_rows * KB // total_blocks
    slot_count = total_blocks * capacity
    per_owner = owned_blocks * capacity
    target = slot_targets(row_blocks, total_blocks, capacity)
    slots = jnp.arange(slot_count, dtype=jnp.int32)

    pair_hot = target[None, :] == slots[:, None]
    row_hot = jnp.any(pair_hot.reshape(slot_count, group_rows, KB), axis=2).astype(jnp.bfloat16)
    pair_hot = pair_hot.astype(jnp.bfloat16)

    centered = (activations - center_bias[None, :]).astype(jnp.bfloat16)
    outgoing = jnp.dot(row_hot, centered, preferred_element_type=jnp.float32).astype(jnp.bfloat16)
    offs_plus = (pick_offsets.reshape(-1, PER) + 1).astype(jnp.bfloat16)
    out_offs_t = lax.dot_general(
        offs_plus, pair_hot, (((0,), (1,)), ((), ())), preferred_element_type=jnp.float32
    ).astype(jnp.int32)
    out_offs = out_offs_t.reshape(PER, owners, per_owner).transpose(1, 0, 2)

    got_offs = lax.all_to_all(out_offs, "lat", split_axis=0, concat_axis=0, tiled=True)
    got_rows = lax.all_to_all(
        outgoing.reshape(owners, per_owner, feature_width),
        "lat",
        split_axis=0,
        concat_axis=0,
        tiled=True,
    )
    got_rows = got_rows.reshape(slot_count, feature_width)
    offs_t = got_offs.transpose(1, 0, 2).reshape(PER, slot_count) - 1

    slot_block = (slots // capacity) % owned_blocks
    col_block = jnp.arange(owned_cols, dtype=jnp.int32) // BLK
    own_col = col_block[:, None] == slot_block[None, :]

    def own_half(full_t):
        parts = full_t.reshape(owned_blocks, BLK, slot_count)
        sel = jnp.arange(owned_blocks, dtype=jnp.int32)[:, None, None] == slot_block[None, None, :]
        return jnp.sum(jnp.where(sel, parts, 0.0), axis=0)

    def widen(narrow_t):
        tiled = jnp.tile(narrow_t, (owned_blocks, 1))
        return jnp.where(own_col, tiled, jnp.zeros_like(tiled))

    partial_t = lax.dot_general(
        encoder_weight, got_rows, (((0,), (1,)), ((), ())), preferred_element_type=jnp.float32
    )
    partial = pick_rows(own_half(partial_t), offs_t)
    summed = butterfly_sum(partial, "row")
    bias_t = own_half(jnp.broadcast_to(encoder_bias[:, None], (owned_cols, slot_count)))
    pre_picked = summed + pick_rows(bias_t, offs_t)
    latent_t = spread_rows(pre_picked, offs_t).astype(jnp.bfloat16)
    latent_wide_t = widen(latent_t)
    decoded = lax.dot_general(
        latent_wide_t, decoder_weight, (((0,), (0,)), ((), ())), preferred_element_type=jnp.float32
    ).astype(jnp.bfloat16)
    returned = lax.all_to_all(
        decoded.reshape(owners, per_owner, feature_width),
        "lat",
        split_axis=0,
        concat_axis=0,
        tiled=True,
    ).reshape(slot_count, feature_width)
    rebuilt = lax.dot_general(
        row_hot, returned, (((0,), (0,)), ((), ())), preferred_element_type=jnp.float32
    )
    recon_error = (center_bias[None, :] + rebuilt) - activations
    loss_part = jnp.sum(recon_error * recon_error, axis=1)
    error_b = recon_error.astype(jnp.bfloat16)
    out_error = jnp.dot(row_hot, error_b, preferred_element_type=jnp.float32).astype(jnp.bfloat16)
    got_error = lax.all_to_all(
        out_error.reshape(owners, per_owner, feature_width),
        "lat",
        split_axis=0,
        concat_axis=0,
        tiled=True,
    ).reshape(slot_count, feature_width)
    decoder_grad = lax.dot_general(
        latent_wide_t, got_error, (((1,), (0,)), ((), ())), preferred_element_type=jnp.float32
    ).astype(jnp.bfloat16)
    dlatent_t = lax.dot_general(
        decoder_weight, got_error, (((1,), (1,)), ((), ())), preferred_element_type=jnp.float32
    )
    dlatent_part = pick_rows(own_half(dlatent_t), offs_t)
    loss_row = jnp.zeros((1, slot_count), jnp.float32).at[0, :group_rows].set(loss_part)
    reduced = butterfly_sum(jnp.concatenate([dlatent_part, loss_row], axis=0), "row")
    dlatent = reduced[:PER]
    loss_total = reduced[PER, :group_rows]
    grad_t = spread_rows(dlatent, offs_t).astype(jnp.bfloat16)
    grad_wide_t = widen(grad_t)
    encoder_grad = lax.dot_general(
        got_rows, grad_wide_t, (((0,), (1,)), ((), ())), preferred_element_type=jnp.float32
    ).astype(jnp.bfloat16)
    bias_grad = jnp.sum(grad_wide_t.astype(jnp.float32), axis=1)
    row_loss = loss_total / D
    return (encoder_grad, decoder_grad, bias_grad, row_loss)


def solution(mesh):
    return jax.shard_map(
        per_device,
        mesh=mesh,
        in_specs=(
            P("lat", "row"),
            P("row"),
            P("row", "lat"),
            P("lat"),
            P("lat", "row"),
            P("lat", None),
            P("lat", None, None),
        ),
        out_specs=(P("row", "lat"), P("lat", "row"), P("lat"), P("lat")),
        check_vma=False,
    )
```

```python
import jax
import jax.numpy as jnp
from jax import lax
from jax.sharding import PartitionSpec as P

D = 8192
BLK = 128
KB = 4
PER = 8


def slot_targets(row_blocks, total_blocks, capacity):
    pair_blocks = row_blocks.reshape(-1)
    onehot = (pair_blocks[:, None] == jnp.arange(total_blocks, dtype=jnp.int32)[None, :]).astype(
        jnp.int32
    )
    before = jnp.cumsum(onehot, axis=0) - onehot
    ranking = jnp.sum(before * onehot, axis=1)
    return pair_blocks * capacity + ranking


def pick_rows(values_t, offsets_t):
    lanes = jnp.arange(BLK, dtype=jnp.int32)
    hit = offsets_t[:, None, :] == lanes[None, :, None]
    return jnp.sum(jnp.where(hit, values_t[None, :, :], 0.0), axis=1)


def spread_rows(picked_t, offsets_t):
    lanes = jnp.arange(BLK, dtype=jnp.int32)[:, None]
    out = jnp.zeros((BLK, picked_t.shape[1]), picked_t.dtype)
    for j in range(PER):
        out = jnp.where(offsets_t[j : j + 1, :] == lanes, picked_t[j : j + 1, :], out)
    return out


def gathered_sum(x, axis):
    return jnp.sum(lax.all_gather(x, axis, axis=0), axis=0)


def per_device(
    activations, center_bias, encoder_weight, encoder_bias, decoder_weight, row_blocks, pick_offsets
):
    group_rows, feature_width = activations.shape
    owners = lax.axis_size("lat")
    owned_blocks = encoder_bias.shape[0] // BLK
    owned_cols = owned_blocks * BLK
    total_blocks = owned_blocks * owners
    capacity = 2 * group_rows * KB // total_blocks
    slot_count = total_blocks * capacity
    per_owner = owned_blocks * capacity
    target = slot_targets(row_blocks, total_blocks, capacity)
    slots = jnp.arange(slot_count, dtype=jnp.int32)

    pair_hot = target[None, :] == slots[:, None]
    row_hot = jnp.any(pair_hot.reshape(slot_count, group_rows, KB), axis=2).astype(jnp.bfloat16)
    pair_hot = pair_hot.astype(jnp.bfloat16)

    centered = (activations - center_bias[None, :]).astype(jnp.bfloat16)
    outgoing = jnp.dot(row_hot, centered, preferred_element_type=jnp.float32).astype(jnp.bfloat16)
    offs_plus = (pick_offsets.reshape(-1, PER) + 1).astype(jnp.bfloat16)
    out_offs_t = lax.dot_general(
        offs_plus, pair_hot, (((0,), (1,)), ((), ())), preferred_element_type=jnp.float32
    ).astype(jnp.int32)
    out_offs = out_offs_t.reshape(PER, owners, per_owner).transpose(1, 0, 2)

    got_offs = lax.all_to_all(out_offs, "lat", split_axis=0, concat_axis=0, tiled=True)
    got_rows = lax.all_to_all(
        outgoing.reshape(owners, per_owner, feature_width),
        "lat",
        split_axis=0,
        concat_axis=0,
        tiled=True,
    )
    got_rows = got_rows.reshape(slot_count, feature_width)
    offs_t = got_offs.transpose(1, 0, 2).reshape(PER, slot_count) - 1

    slot_block = (slots // capacity) % owned_blocks
    col_block = jnp.arange(owned_cols, dtype=jnp.int32) // BLK
    own_col = col_block[:, None] == slot_block[None, :]

    def own_half(full_t):
        parts = full_t.reshape(owned_blocks, BLK, slot_count)
        sel = jnp.arange(owned_blocks, dtype=jnp.int32)[:, None, None] == slot_block[None, None, :]
        return jnp.sum(jnp.where(sel, parts, 0.0), axis=0)

    def widen(narrow_t):
        tiled = jnp.tile(narrow_t, (owned_blocks, 1))
        return jnp.where(own_col, tiled, jnp.zeros_like(tiled))

    partial_t = lax.dot_general(
        encoder_weight, got_rows, (((0,), (1,)), ((), ())), preferred_element_type=jnp.float32
    )
    partial = pick_rows(own_half(partial_t), offs_t)
    summed = gathered_sum(partial, "row")
    bias_t = own_half(jnp.broadcast_to(encoder_bias[:, None], (owned_cols, slot_count)))
    pre_picked = summed + pick_rows(bias_t, offs_t)
    latent_t = spread_rows(pre_picked, offs_t).astype(jnp.bfloat16)
    latent_wide_t = widen(latent_t)
    decoded = lax.dot_general(
        latent_wide_t, decoder_weight, (((0,), (0,)), ((), ())), preferred_element_type=jnp.float32
    ).astype(jnp.bfloat16)
    returned = lax.all_to_all(
        decoded.reshape(owners, per_owner, feature_width),
        "lat",
        split_axis=0,
        concat_axis=0,
        tiled=True,
    ).reshape(slot_count, feature_width)
    rebuilt = lax.dot_general(
        row_hot, returned, (((0,), (0,)), ((), ())), preferred_element_type=jnp.float32
    )
    recon_error = (center_bias[None, :] + rebuilt) - activations
    loss_part = jnp.sum(recon_error * recon_error, axis=1)
    error_b = recon_error.astype(jnp.bfloat16)
    out_error = jnp.dot(row_hot, error_b, preferred_element_type=jnp.float32).astype(jnp.bfloat16)
    got_error = lax.all_to_all(
        out_error.reshape(owners, per_owner, feature_width),
        "lat",
        split_axis=0,
        concat_axis=0,
        tiled=True,
    ).reshape(slot_count, feature_width)
    decoder_grad = lax.dot_general(
        latent_wide_t, got_error, (((1,), (0,)), ((), ())), preferred_element_type=jnp.float32
    ).astype(jnp.bfloat16)
    dlatent_t = lax.dot_general(
        decoder_weight, got_error, (((1,), (1,)), ((), ())), preferred_element_type=jnp.float32
    )
    dlatent_part = pick_rows(own_half(dlatent_t), offs_t)
    loss_row = jnp.zeros((1, slot_count), jnp.float32).at[0, :group_rows].set(loss_part)
    reduced = gathered_sum(jnp.concatenate([dlatent_part, loss_row], axis=0), "row")
    dlatent = reduced[:PER]
    loss_total = reduced[PER, :group_rows]
    grad_t = spread_rows(dlatent, offs_t).astype(jnp.bfloat16)
    grad_wide_t = widen(grad_t)
    encoder_grad = lax.dot_general(
        got_rows, grad_wide_t, (((0,), (1,)), ((), ())), preferred_element_type=jnp.float32
    ).astype(jnp.bfloat16)
    bias_grad = jnp.sum(grad_wide_t.astype(jnp.float32), axis=1)
    row_loss = loss_total / D
    return (encoder_grad, decoder_grad, bias_grad, row_loss)


def solution(mesh):
    return jax.shard_map(
        per_device,
        mesh=mesh,
        in_specs=(
            P("lat", "row"),
            P("row"),
            P("row", "lat"),
            P("lat"),
            P("lat", "row"),
            P("lat", None),
            P("lat", None, None),
        ),
        out_specs=(P("row", "lat"), P("lat", "row"), P("lat"), P("lat")),
        check_vma=False,
    )
```

```python
import jax
import jax.numpy as jnp
from jax import lax
from jax.sharding import PartitionSpec as P


D = 8192
BLK = 128
KB = 4
PER = 8
RANK_PARTS = (4, 8)


def slot_ranks(row_blocks, total_blocks):
    pair_blocks = row_blocks.reshape(-1)
    onehot = (pair_blocks[:, None] == jnp.arange(total_blocks, dtype=jnp.int32)[None, :]).astype(
        jnp.int32
    )
    before = jnp.cumsum(onehot, axis=0) - onehot
    return pair_blocks, jnp.sum(before * onehot, axis=1)


def pick_rows(values_t, offsets_t):
    lanes = jnp.arange(BLK, dtype=jnp.int32)
    hit = offsets_t[:, None, :] == lanes[None, :, None]
    return jnp.sum(jnp.where(hit, values_t[None, :, :], 0.0), axis=1)


def spread_rows(picked_t, offsets_t):
    lanes = jnp.arange(BLK, dtype=jnp.int32)[:, None]
    out = jnp.zeros((BLK, picked_t.shape[1]), picked_t.dtype)
    for j in range(PER):
        out = jnp.where(offsets_t[j : j + 1, :] == lanes, picked_t[j : j + 1, :], out)
    return out


def butterfly_sum(x, axis):
    size = lax.axis_size(axis)
    step = 1
    while step < size:
        other = lax.ppermute(x, axis, perm=[(i, i ^ step) for i in range(size)])
        x = x + other
        step *= 2
    return x


def exchange(x, owners):
    rows = x.shape[0]
    return lax.all_to_all(
        x.reshape((owners, rows // owners) + x.shape[1:]), "lat", split_axis=0, concat_axis=0, tiled=True
    ).reshape(x.shape)


def device_step(
    activations, center_bias, encoder_weight, encoder_bias, decoder_weight, row_blocks, pick_offsets
):
    group_rows, feature_width = activations.shape
    owners = lax.axis_size("lat")
    owned_blocks = encoder_bias.shape[0] // BLK
    owned_cols = owned_blocks * BLK
    total_blocks = owned_blocks * owners
    capacity = 2 * group_rows * KB // total_blocks
    slot_count = total_blocks * capacity
    per_owner = owned_blocks * capacity
    assert sum(RANK_PARTS) == capacity
    bases = [owned_blocks * sum(RANK_PARTS[:h]) for h in range(len(RANK_PARTS))]
    pair_blocks, rank = slot_ranks(row_blocks, total_blocks)
    owner_of, block_in = pair_blocks // owned_blocks, pair_blocks % owned_blocks
    second = rank >= RANK_PARTS[0]
    in_chunk = jnp.where(second, rank - RANK_PARTS[0], rank)
    chunk_len = jnp.where(second, RANK_PARTS[1], RANK_PARTS[0])
    chunk_base = jnp.where(second, bases[1], bases[0])
    target = owner_of * per_owner + chunk_base + block_in * chunk_len + in_chunk
    slots = jnp.arange(slot_count, dtype=jnp.int32)

    pair_hot = target[None, :] == slots[:, None]
    row_hot = jnp.any(pair_hot.reshape(slot_count, group_rows, KB), axis=2).astype(jnp.bfloat16)
    pair_hot = pair_hot.astype(jnp.bfloat16)
    row_hot_owner = row_hot.reshape(owners, per_owner, group_rows)

    centered = (activations - center_bias[None, :]).astype(jnp.bfloat16)
    offs_plus = (pick_offsets.reshape(-1, PER) + 1).astype(jnp.bfloat16)
    out_offs_t = lax.dot_general(
        offs_plus, pair_hot, (((0,), (1,)), ((), ())), preferred_element_type=jnp.float32
    ).astype(jnp.int32)
    out_offs = out_offs_t.reshape(PER, owners, per_owner).transpose(1, 0, 2)
    got_offs = lax.all_to_all(out_offs, "lat", split_axis=0, concat_axis=0, tiled=True)
    col_block = jnp.arange(owned_cols, dtype=jnp.int32) // BLK

    def own_half(full_t, slot_block):
        parts = full_t.reshape(owned_blocks, BLK, slot_block.shape[0])
        sel = jnp.arange(owned_blocks, dtype=jnp.int32)[:, None, None] == slot_block[None, None, :]
        return jnp.sum(jnp.where(sel, parts, 0.0), axis=0)

    def widen(narrow_t, slot_block):
        tiled = jnp.tile(narrow_t, (owned_blocks, 1))
        return jnp.where(col_block[:, None] == slot_block[None, :], tiled, jnp.zeros_like(tiled))

    got_rows, offs_t, latent_wide_t, blocks_of, rebuilt = [], [], [], [], None
    for h, part in enumerate(RANK_PARTS):
        width = owned_blocks * part
        chunk_slots = owners * width
        slot_block = (jnp.arange(chunk_slots, dtype=jnp.int32) // part) % owned_blocks
        hot_h = row_hot_owner[:, bases[h] : bases[h] + width].reshape(chunk_slots, group_rows)
        outgoing = jnp.dot(hot_h, centered, preferred_element_type=jnp.float32).astype(jnp.bfloat16)
        rows_h = exchange(outgoing, owners)
        offs_h = got_offs[:, :, bases[h] : bases[h] + width].transpose(1, 0, 2)
        offs_h = offs_h.reshape(PER, chunk_slots) - 1
        partial_t = lax.dot_general(
            encoder_weight, rows_h, (((0,), (1,)), ((), ())), preferred_element_type=jnp.float32
        )
        summed = butterfly_sum(pick_rows(own_half(partial_t, slot_block), offs_h), "row")
        bias_t = own_half(jnp.broadcast_to(encoder_bias[:, None], (owned_cols, chunk_slots)), slot_block)
        pre_picked = summed + pick_rows(bias_t, offs_h)
        latent_h = widen(spread_rows(pre_picked, offs_h).astype(jnp.bfloat16), slot_block)
        decoded = lax.dot_general(
            latent_h, decoder_weight, (((0,), (0,)), ((), ())), preferred_element_type=jnp.float32
        ).astype(jnp.bfloat16)
        returned = exchange(decoded, owners)
        term = lax.dot_general(
            hot_h, returned, (((0,), (0,)), ((), ())), preferred_element_type=jnp.float32
        )
        rebuilt = term if rebuilt is None else rebuilt + term
        got_rows.append(rows_h)
        offs_t.append(offs_h)
        latent_wide_t.append(latent_h)
        blocks_of.append(slot_block)

    recon_error = (center_bias[None, :] + rebuilt) - activations
    loss_part = jnp.sum(recon_error * recon_error, axis=1)
    error_b = recon_error.astype(jnp.bfloat16)
    out_error = jnp.dot(row_hot, error_b, preferred_element_type=jnp.float32).astype(jnp.bfloat16)
    got_error = exchange(out_error, owners).reshape(owners, per_owner, feature_width)
    errors = [
        got_error[:, bases[h] : bases[h] + owned_blocks * part].reshape(-1, feature_width)
        for h, part in enumerate(RANK_PARTS)
    ]

    decoder_grad = None
    dlatent_parts = []
    for h in range(len(RANK_PARTS)):
        term = lax.dot_general(
            latent_wide_t[h], errors[h], (((1,), (0,)), ((), ())), preferred_element_type=jnp.float32
        )
        decoder_grad = term if decoder_grad is None else decoder_grad + term
        dlatent_t = lax.dot_general(
            decoder_weight, errors[h], (((1,), (1,)), ((), ())), preferred_element_type=jnp.float32
        )
        dlatent_parts.append(pick_rows(own_half(dlatent_t, blocks_of[h]), offs_t[h]))
    decoder_grad = decoder_grad.astype(jnp.bfloat16)
    flat = jnp.concatenate([p.reshape(-1) for p in dlatent_parts] + [loss_part])
    reduced = butterfly_sum(flat, "row")
    loss_total = reduced[PER * slot_count :]

    encoder_grad, bias_grad = None, None
    start = 0
    for h in range(len(RANK_PARTS)):
        size = offs_t[h].size
        dl_h = reduced[start : start + size].reshape(offs_t[h].shape)
        start += size
        grad_h = widen(spread_rows(dl_h, offs_t[h]).astype(jnp.bfloat16), blocks_of[h])
        term = lax.dot_general(
            got_rows[h], grad_h, (((0,), (1,)), ((), ())), preferred_element_type=jnp.float32
        )
        bias_term = jnp.sum(grad_h.astype(jnp.float32), axis=1)
        encoder_grad = term if encoder_grad is None else encoder_grad + term
        bias_grad = bias_term if bias_grad is None else bias_grad + bias_term
    encoder_grad = encoder_grad.astype(jnp.bfloat16)
    row_loss = loss_total / D
    return (encoder_grad, decoder_grad, bias_grad, row_loss)


def solution(mesh):
    return jax.shard_map(
        device_step,
        mesh=mesh,
        in_specs=(
            P("lat", "row"),
            P("row"),
            P("row", "lat"),
            P("lat"),
            P("lat", "row"),
            P("lat", None),
            P("lat", None, None),
        ),
        out_specs=(P("row", "lat"), P("lat", "row"), P("lat"), P("lat")),
        check_vma=False,
    )
```

```python
import jax
import jax.numpy as jnp
from jax import lax
from jax.sharding import PartitionSpec as P

D = 8192
BLK = 128
KB = 4
PER = 8


def slot_targets(row_blocks, total_blocks, capacity):
    pair_blocks = row_blocks.reshape(-1)
    onehot = (pair_blocks[:, None] == jnp.arange(total_blocks, dtype=jnp.int32)[None, :]).astype(
        jnp.int32
    )
    before = jnp.cumsum(onehot, axis=0) - onehot
    ranking = jnp.sum(before * onehot, axis=1)
    return pair_blocks * capacity + ranking


def pick_rows(values_t, offsets_t):
    lanes = jnp.arange(BLK, dtype=jnp.int32)
    hit = offsets_t[:, None, :] == lanes[None, :, None]
    return jnp.sum(jnp.where(hit, values_t[None, :, :], 0.0), axis=1)


def spread_rows(picked_t, offsets_t):
    lanes = jnp.arange(BLK, dtype=jnp.int32)[:, None]
    out = jnp.zeros((BLK, picked_t.shape[1]), picked_t.dtype)
    for j in range(PER):
        out = jnp.where(offsets_t[j : j + 1, :] == lanes, picked_t[j : j + 1, :], out)
    return out


def butterfly_sum(x, axis):
    size = lax.axis_size(axis)
    step = 1
    while step < size:
        other = lax.ppermute(x, axis, perm=[(i, i ^ step) for i in range(size)])
        x = x + other
        step *= 2
    return x


def per_device(
    activations, center_bias, encoder_weight, encoder_bias, decoder_weight, row_blocks, pick_offsets
):
    group_rows, feature_width = activations.shape
    owners = lax.axis_size("lat")
    owned_blocks = encoder_bias.shape[0] // BLK
    owned_cols = owned_blocks * BLK
    total_blocks = owned_blocks * owners
    capacity = 2 * group_rows * KB // total_blocks
    slot_count = total_blocks * capacity
    per_owner = owned_blocks * capacity
    target = slot_targets(row_blocks, total_blocks, capacity)
    slots = jnp.arange(slot_count, dtype=jnp.int32)

    pair_hot = target[None, :] == slots[:, None]
    row_hot = jnp.any(pair_hot.reshape(slot_count, group_rows, KB), axis=2).astype(jnp.bfloat16)
    pair_hot = pair_hot.astype(jnp.bfloat16)

    centered = (activations - center_bias[None, :]).astype(jnp.bfloat16)
    outgoing = jnp.dot(row_hot, centered, preferred_element_type=jnp.float32).astype(jnp.bfloat16)
    offs_plus = (pick_offsets.reshape(-1, PER) + 1).astype(jnp.bfloat16)
    out_offs = jnp.dot(pair_hot, offs_plus, preferred_element_type=jnp.float32).astype(jnp.bfloat16)
    payload = jnp.concatenate(
        [outgoing, out_offs, jnp.zeros((slot_count, BLK - PER), jnp.bfloat16)], axis=1
    )
    got = lax.all_to_all(
        payload.reshape(owners, per_owner, feature_width + BLK),
        "lat",
        split_axis=0,
        concat_axis=0,
        tiled=True,
    ).reshape(slot_count, feature_width + BLK)
    got_rows = got[:, :feature_width]
    offs_t = got[:, feature_width : feature_width + PER].astype(jnp.int32).T - 1

    slot_block = (slots // capacity) % owned_blocks
    col_block = jnp.arange(owned_cols, dtype=jnp.int32) // BLK
    own_col = col_block[:, None] == slot_block[None, :]

    def own_half(full_t):
        parts = full_t.reshape(owned_blocks, BLK, slot_count)
        sel = jnp.arange(owned_blocks, dtype=jnp.int32)[:, None, None] == slot_block[None, None, :]
        return jnp.sum(jnp.where(sel, parts, 0.0), axis=0)

    def widen(narrow_t):
        tiled = jnp.tile(narrow_t, (owned_blocks, 1))
        return jnp.where(own_col, tiled, jnp.zeros_like(tiled))

    partial_t = lax.dot_general(
        encoder_weight, got_rows, (((0,), (1,)), ((), ())), preferred_element_type=jnp.float32
    )
    partial = pick_rows(own_half(partial_t), offs_t)
    summed = butterfly_sum(partial, "row")
    bias_t = own_half(jnp.broadcast_to(encoder_bias[:, None], (owned_cols, slot_count)))
    pre_picked = summed + pick_rows(bias_t, offs_t)
    latent_t = spread_rows(pre_picked, offs_t).astype(jnp.bfloat16)
    latent_wide_t = widen(latent_t)
    decoded = lax.dot_general(
        latent_wide_t, decoder_weight, (((0,), (0,)), ((), ())), preferred_element_type=jnp.float32
    ).astype(jnp.bfloat16)
    returned = lax.all_to_all(
        decoded.reshape(owners, per_owner, feature_width),
        "lat",
        split_axis=0,
        concat_axis=0,
        tiled=True,
    ).reshape(slot_count, feature_width)
    rebuilt = lax.dot_general(
        row_hot, returned, (((0,), (0,)), ((), ())), preferred_element_type=jnp.float32
    )
    recon_error = (center_bias[None, :] + rebuilt) - activations
    loss_part = jnp.sum(recon_error * recon_error, axis=1)
    error_b = recon_error.astype(jnp.bfloat16)
    out_error = jnp.dot(row_hot, error_b, preferred_element_type=jnp.float32).astype(jnp.bfloat16)
    got_error = lax.all_to_all(
        out_error.reshape(owners, per_owner, feature_width),
        "lat",
        split_axis=0,
        concat_axis=0,
        tiled=True,
    ).reshape(slot_count, feature_width)
    decoder_grad = lax.dot_general(
        latent_wide_t, got_error, (((1,), (0,)), ((), ())), preferred_element_type=jnp.float32
    ).astype(jnp.bfloat16)
    dlatent_t = lax.dot_general(
        decoder_weight, got_error, (((1,), (1,)), ((), ())), preferred_element_type=jnp.float32
    )
    dlatent_part = pick_rows(own_half(dlatent_t), offs_t)
    loss_row = jnp.zeros((1, slot_count), jnp.float32).at[0, :group_rows].set(loss_part)
    reduced = butterfly_sum(jnp.concatenate([dlatent_part, loss_row], axis=0), "row")
    dlatent = reduced[:PER]
    loss_total = reduced[PER, :group_rows]
    grad_t = spread_rows(dlatent, offs_t).astype(jnp.bfloat16)
    grad_wide_t = widen(grad_t)
    encoder_grad = lax.dot_general(
        got_rows, grad_wide_t, (((0,), (1,)), ((), ())), preferred_element_type=jnp.float32
    ).astype(jnp.bfloat16)
    bias_grad = jnp.sum(grad_wide_t.astype(jnp.float32), axis=1)
    row_loss = loss_total / D
    return (encoder_grad, decoder_grad, bias_grad, row_loss)


def solution(mesh):
    return jax.shard_map(
        per_device,
        mesh=mesh,
        in_specs=(
            P("lat", "row"),
            P("row"),
            P("row", "lat"),
            P("lat"),
            P("lat", "row"),
            P("lat", None),
            P("lat", None, None),
        ),
        out_specs=(P("row", "lat"), P("lat", "row"), P("lat"), P("lat")),
        check_vma=False,
    )
```

```python
import jax
import jax.numpy as jnp
from jax import lax
from jax.sharding import PartitionSpec as P

D = 8192
BLK = 128
KB = 4
PER = 8


def slot_targets(row_blocks, total_blocks, capacity):
    pair_blocks = row_blocks.reshape(-1)
    onehot = (pair_blocks[:, None] == jnp.arange(total_blocks, dtype=jnp.int32)[None, :]).astype(
        jnp.int32
    )
    before = jnp.cumsum(onehot, axis=0) - onehot
    ranking = jnp.sum(before * onehot, axis=1)
    return pair_blocks * capacity + ranking


def pick_rows(values_t, offsets_t):
    lanes = jnp.arange(BLK, dtype=jnp.int32)
    hit = offsets_t[:, None, :] == lanes[None, :, None]
    return jnp.sum(jnp.where(hit, values_t[None, :, :], 0.0), axis=1)


def spread_rows(picked_t, offsets_t):
    lanes = jnp.arange(BLK, dtype=jnp.int32)[:, None]
    out = jnp.zeros((BLK, picked_t.shape[1]), picked_t.dtype)
    for j in range(PER):
        out = jnp.where(offsets_t[j : j + 1, :] == lanes, picked_t[j : j + 1, :], out)
    return out


def butterfly_sum(x, axis):
    size = lax.axis_size(axis)
    step = 1
    while step < size:
        other = lax.ppermute(x, axis, perm=[(i, i ^ step) for i in range(size)])
        x = x + other
        step *= 2
    return x


def per_device(
    activations, center_bias, encoder_weight, encoder_bias, decoder_weight, row_blocks, pick_offsets
):
    group_rows, feature_width = activations.shape
    owners = lax.axis_size("lat")
    owned_blocks = encoder_bias.shape[0] // BLK
    owned_cols = owned_blocks * BLK
    total_blocks = owned_blocks * owners
    capacity = 2 * group_rows * KB // total_blocks
    slot_count = total_blocks * capacity
    per_owner = owned_blocks * capacity
    target = slot_targets(row_blocks, total_blocks, capacity)
    slots = jnp.arange(slot_count, dtype=jnp.int32)

    pair_hot = target[None, :] == slots[:, None]
    row_hot = jnp.any(pair_hot.reshape(slot_count, group_rows, KB), axis=2).astype(jnp.bfloat16)
    pair_hot = pair_hot.astype(jnp.bfloat16)

    centered = (activations - center_bias[None, :]).astype(jnp.bfloat16)
    offs_plus = (pick_offsets.reshape(-1, PER) + 1).astype(jnp.bfloat16)
    pair_data = jnp.concatenate(
        [
            jnp.repeat(centered, KB, axis=0),
            offs_plus,
            jnp.zeros((group_rows * KB, BLK - PER), jnp.bfloat16),
        ],
        axis=1,
    )
    payload = jnp.dot(pair_hot, pair_data, preferred_element_type=jnp.float32).astype(jnp.bfloat16)
    got = lax.all_to_all(
        payload.reshape(owners, per_owner, feature_width + BLK),
        "lat",
        split_axis=0,
        concat_axis=0,
        tiled=True,
    ).reshape(slot_count, feature_width + BLK)
    got_rows = got[:, :feature_width]
    offs_t = got[:, feature_width : feature_width + PER].astype(jnp.int32).T - 1

    slot_block = (slots // capacity) % owned_blocks
    col_block = jnp.arange(owned_cols, dtype=jnp.int32) // BLK
    own_col = col_block[:, None] == slot_block[None, :]

    def own_half(full_t):
        parts = full_t.reshape(owned_blocks, BLK, slot_count)
        sel = jnp.arange(owned_blocks, dtype=jnp.int32)[:, None, None] == slot_block[None, None, :]
        return jnp.sum(jnp.where(sel, parts, 0.0), axis=0)

    def widen(narrow_t):
        tiled = jnp.tile(narrow_t, (owned_blocks, 1))
        return jnp.where(own_col, tiled, jnp.zeros_like(tiled))

    partial_t = lax.dot_general(
        encoder_weight, got_rows, (((0,), (1,)), ((), ())), preferred_element_type=jnp.float32
    )
    partial = pick_rows(own_half(partial_t), offs_t)
    summed = butterfly_sum(partial, "row")
    bias_t = own_half(jnp.broadcast_to(encoder_bias[:, None], (owned_cols, slot_count)))
    pre_picked = summed + pick_rows(bias_t, offs_t)
    latent_t = spread_rows(pre_picked, offs_t).astype(jnp.bfloat16)
    latent_wide_t = widen(latent_t)
    decoded = lax.dot_general(
        latent_wide_t, decoder_weight, (((0,), (0,)), ((), ())), preferred_element_type=jnp.float32
    ).astype(jnp.bfloat16)
    returned = lax.all_to_all(
        decoded.reshape(owners, per_owner, feature_width),
        "lat",
        split_axis=0,
        concat_axis=0,
        tiled=True,
    ).reshape(slot_count, feature_width)
    rebuilt = lax.dot_general(
        row_hot, returned, (((0,), (0,)), ((), ())), preferred_element_type=jnp.float32
    )
    recon_error = (center_bias[None, :] + rebuilt) - activations
    loss_part = jnp.sum(recon_error * recon_error, axis=1)
    error_b = recon_error.astype(jnp.bfloat16)
    out_error = jnp.dot(row_hot, error_b, preferred_element_type=jnp.float32).astype(jnp.bfloat16)
    got_error = lax.all_to_all(
        out_error.reshape(owners, per_owner, feature_width),
        "lat",
        split_axis=0,
        concat_axis=0,
        tiled=True,
    ).reshape(slot_count, feature_width)
    decoder_grad = lax.dot_general(
        latent_wide_t, got_error, (((1,), (0,)), ((), ())), preferred_element_type=jnp.float32
    ).astype(jnp.bfloat16)
    dlatent_t = lax.dot_general(
        decoder_weight, got_error, (((1,), (1,)), ((), ())), preferred_element_type=jnp.float32
    )
    dlatent_part = pick_rows(own_half(dlatent_t), offs_t)
    loss_row = jnp.zeros((1, slot_count), jnp.float32).at[0, :group_rows].set(loss_part)
    reduced = butterfly_sum(jnp.concatenate([dlatent_part, loss_row], axis=0), "row")
    dlatent = reduced[:PER]
    loss_total = reduced[PER, :group_rows]
    grad_t = spread_rows(dlatent, offs_t).astype(jnp.bfloat16)
    grad_wide_t = widen(grad_t)
    encoder_grad = lax.dot_general(
        got_rows, grad_wide_t, (((0,), (1,)), ((), ())), preferred_element_type=jnp.float32
    ).astype(jnp.bfloat16)
    bias_grad = jnp.sum(grad_wide_t.astype(jnp.float32), axis=1)
    row_loss = loss_total / D
    return (encoder_grad, decoder_grad, bias_grad, row_loss)


def solution(mesh):
    return jax.shard_map(
        per_device,
        mesh=mesh,
        in_specs=(
            P("lat", "row"),
            P("row"),
            P("row", "lat"),
            P("lat"),
            P("lat", "row"),
            P("lat", None),
            P("lat", None, None),
        ),
        out_specs=(P("row", "lat"), P("lat", "row"), P("lat"), P("lat")),
        check_vma=False,
    )
```

```python
import jax
import jax.numpy as jnp
from jax import lax
from jax.sharding import PartitionSpec as P

D = 8192
BLK = 128
KB = 4
PER = 8


def slot_targets(row_blocks, total_blocks, capacity):
    pair_blocks = row_blocks.reshape(-1)
    onehot = (pair_blocks[:, None] == jnp.arange(total_blocks, dtype=jnp.int32)[None, :]).astype(
        jnp.int32
    )
    before = jnp.cumsum(onehot, axis=0) - onehot
    ranking = jnp.sum(before * onehot, axis=1)
    return pair_blocks * capacity + ranking


def pick_rows(values_t, offsets_t):
    lanes = jnp.arange(BLK, dtype=jnp.int32)
    hit = offsets_t[:, None, :] == lanes[None, :, None]
    return jnp.sum(jnp.where(hit, values_t[None, :, :], 0.0), axis=1)


def spread_rows(picked_t, offsets_t):
    lanes = jnp.arange(BLK, dtype=jnp.int32)[:, None]
    out = jnp.zeros((BLK, picked_t.shape[1]), picked_t.dtype)
    for j in range(PER):
        out = jnp.where(offsets_t[j : j + 1, :] == lanes, picked_t[j : j + 1, :], out)
    return out


def butterfly_sum(x, axis):
    size = lax.axis_size(axis)
    step = 1
    while step < size:
        other = lax.ppermute(x, axis, perm=[(i, i ^ step) for i in range(size)])
        x = x + other
        step *= 2
    return x


def per_device(
    activations, center_bias, encoder_weight, encoder_bias, decoder_weight, row_blocks, pick_offsets
):
    group_rows, feature_width = activations.shape
    owners = lax.axis_size("lat")
    owned_blocks = encoder_bias.shape[0] // BLK
    owned_cols = owned_blocks * BLK
    total_blocks = owned_blocks * owners
    capacity = 2 * group_rows * KB // total_blocks
    slot_count = total_blocks * capacity
    per_owner = owned_blocks * capacity
    target = slot_targets(row_blocks, total_blocks, capacity)
    slots = jnp.arange(slot_count, dtype=jnp.int32)

    pair_hot = target[None, :] == slots[:, None]
    row_hot = jnp.any(pair_hot.reshape(slot_count, group_rows, KB), axis=2).astype(jnp.bfloat16)
    pair_hot = pair_hot.astype(jnp.bfloat16)

    centered = (activations - center_bias[None, :]).astype(jnp.bfloat16)
    outgoing = jnp.dot(row_hot, centered, preferred_element_type=jnp.float32).astype(jnp.bfloat16)
    offs_plus = (pick_offsets.reshape(-1, PER) + 1).astype(jnp.bfloat16)
    out_offs_t = lax.dot_general(
        offs_plus, pair_hot, (((0,), (1,)), ((), ())), preferred_element_type=jnp.float32
    ).astype(jnp.int32)
    out_offs = out_offs_t.reshape(PER, owners, per_owner).transpose(1, 0, 2)

    got_rows = lax.all_to_all(
        outgoing.reshape(owners, per_owner, feature_width),
        "lat",
        split_axis=0,
        concat_axis=0,
        tiled=True,
    )
    got_rows = got_rows.reshape(slot_count, feature_width)
    after_rows = (got_rows[0, 0] * 0).astype(jnp.int32)
    got_offs = lax.all_to_all(out_offs + after_rows, "lat", split_axis=0, concat_axis=0, tiled=True)
    offs_t = got_offs.transpose(1, 0, 2).reshape(PER, slot_count) - 1

    slot_block = (slots // capacity) % owned_blocks
    col_block = jnp.arange(owned_cols, dtype=jnp.int32) // BLK
    own_col = col_block[:, None] == slot_block[None, :]

    def own_half(full_t):
        parts = full_t.reshape(owned_blocks, BLK, slot_count)
        sel = jnp.arange(owned_blocks, dtype=jnp.int32)[:, None, None] == slot_block[None, None, :]
        return jnp.sum(jnp.where(sel, parts, 0.0), axis=0)

    def widen(narrow_t):
        tiled = jnp.tile(narrow_t, (owned_blocks, 1))
        return jnp.where(own_col, tiled, jnp.zeros_like(tiled))

    partial_t = lax.dot_general(
        encoder_weight, got_rows, (((0,), (1,)), ((), ())), preferred_element_type=jnp.float32
    )
    partial = pick_rows(own_half(partial_t), offs_t)
    summed = butterfly_sum(partial, "row")
    bias_t = own_half(jnp.broadcast_to(encoder_bias[:, None], (owned_cols, slot_count)))
    pre_picked = summed + pick_rows(bias_t, offs_t)
    latent_t = spread_rows(pre_picked, offs_t).astype(jnp.bfloat16)
    latent_wide_t = widen(latent_t)
    decoded = lax.dot_general(
        latent_wide_t, decoder_weight, (((0,), (0,)), ((), ())), preferred_element_type=jnp.float32
    ).astype(jnp.bfloat16)
    returned = lax.all_to_all(
        decoded.reshape(owners, per_owner, feature_width),
        "lat",
        split_axis=0,
        concat_axis=0,
        tiled=True,
    ).reshape(slot_count, feature_width)
    rebuilt = lax.dot_general(
        row_hot, returned, (((0,), (0,)), ((), ())), preferred_element_type=jnp.float32
    )
    recon_error = (center_bias[None, :] + rebuilt) - activations
    loss_part = jnp.sum(recon_error * recon_error, axis=1)
    error_b = recon_error.astype(jnp.bfloat16)
    out_error = jnp.dot(row_hot, error_b, preferred_element_type=jnp.float32).astype(jnp.bfloat16)
    got_error = lax.all_to_all(
        out_error.reshape(owners, per_owner, feature_width),
        "lat",
        split_axis=0,
        concat_axis=0,
        tiled=True,
    ).reshape(slot_count, feature_width)
    decoder_grad = lax.dot_general(
        latent_wide_t, got_error, (((1,), (0,)), ((), ())), preferred_element_type=jnp.float32
    ).astype(jnp.bfloat16)
    dlatent_t = lax.dot_general(
        decoder_weight, got_error, (((1,), (1,)), ((), ())), preferred_element_type=jnp.float32
    )
    dlatent_part = pick_rows(own_half(dlatent_t), offs_t)
    loss_row = jnp.zeros((1, slot_count), jnp.float32).at[0, :group_rows].set(loss_part)
    reduced = butterfly_sum(jnp.concatenate([dlatent_part, loss_row], axis=0), "row")
    dlatent = reduced[:PER]
    loss_total = reduced[PER, :group_rows]
    grad_t = spread_rows(dlatent, offs_t).astype(jnp.bfloat16)
    grad_wide_t = widen(grad_t)
    encoder_grad = lax.dot_general(
        got_rows, grad_wide_t, (((0,), (1,)), ((), ())), preferred_element_type=jnp.float32
    ).astype(jnp.bfloat16)
    bias_grad = jnp.sum(grad_wide_t.astype(jnp.float32), axis=1)
    row_loss = loss_total / D
    return (encoder_grad, decoder_grad, bias_grad, row_loss)


def solution(mesh):
    return jax.shard_map(
        per_device,
        mesh=mesh,
        in_specs=(
            P("lat", "row"),
            P("row"),
            P("row", "lat"),
            P("lat"),
            P("lat", "row"),
            P("lat", None),
            P("lat", None, None),
        ),
        out_specs=(P("row", "lat"), P("lat", "row"), P("lat"), P("lat")),
        check_vma=False,
    )
```

```python
import jax
import jax.numpy as jnp
from jax import lax
from jax.sharding import PartitionSpec as P

D = 8192
BLK = 128
KB = 4
PER = 8


def slot_targets(row_blocks, total_blocks, capacity):
    pair_blocks = row_blocks.reshape(-1)
    onehot = (pair_blocks[:, None] == jnp.arange(total_blocks, dtype=jnp.int32)[None, :]).astype(
        jnp.int32
    )
    before = jnp.cumsum(onehot, axis=0) - onehot
    ranking = jnp.sum(before * onehot, axis=1)
    return pair_blocks * capacity + ranking


def pick_rows(values_t, offsets_t):
    lanes = jnp.arange(BLK, dtype=jnp.int32)
    hit = offsets_t[:, None, :] == lanes[None, :, None]
    return jnp.sum(jnp.where(hit, values_t[None, :, :], 0.0), axis=1)


def spread_rows(picked_t, offsets_t):
    lanes = jnp.arange(BLK, dtype=jnp.int32)[:, None]
    out = jnp.zeros((BLK, picked_t.shape[1]), picked_t.dtype)
    for j in range(PER):
        out = jnp.where(offsets_t[j : j + 1, :] == lanes, picked_t[j : j + 1, :], out)
    return out


def butterfly_sum(x, axis):
    size = lax.axis_size(axis)
    step = size // 2
    while step >= 1:
        other = lax.ppermute(x, axis, perm=[(i, i ^ step) for i in range(size)])
        x = x + other
        step //= 2
    return x


def per_device(
    activations, center_bias, encoder_weight, encoder_bias, decoder_weight, row_blocks, pick_offsets
):
    group_rows, feature_width = activations.shape
    owners = lax.axis_size("lat")
    owned_blocks = encoder_bias.shape[0] // BLK
    owned_cols = owned_blocks * BLK
    total_blocks = owned_blocks * owners
    capacity = 2 * group_rows * KB // total_blocks
    slot_count = total_blocks * capacity
    per_owner = owned_blocks * capacity
    target = slot_targets(row_blocks, total_blocks, capacity)
    slots = jnp.arange(slot_count, dtype=jnp.int32)

    pair_hot = target[None, :] == slots[:, None]
    row_hot = jnp.any(pair_hot.reshape(slot_count, group_rows, KB), axis=2).astype(jnp.bfloat16)
    pair_hot = pair_hot.astype(jnp.bfloat16)

    centered = (activations - center_bias[None, :]).astype(jnp.bfloat16)
    outgoing = jnp.dot(row_hot, centered, preferred_element_type=jnp.float32).astype(jnp.bfloat16)
    offs_plus = (pick_offsets.reshape(-1, PER) + 1).astype(jnp.bfloat16)
    out_offs_t = lax.dot_general(
        offs_plus, pair_hot, (((0,), (1,)), ((), ())), preferred_element_type=jnp.float32
    ).astype(jnp.int32)
    out_offs = out_offs_t.reshape(PER, owners, per_owner).transpose(1, 0, 2)

    got_offs = lax.all_to_all(out_offs, "lat", split_axis=0, concat_axis=0, tiled=True)
    got_rows = lax.all_to_all(
        outgoing.reshape(owners, per_owner, feature_width),
        "lat",
        split_axis=0,
        concat_axis=0,
        tiled=True,
    )
    got_rows = got_rows.reshape(slot_count, feature_width)
    offs_t = got_offs.transpose(1, 0, 2).reshape(PER, slot_count) - 1

    slot_block = (slots // capacity) % owned_blocks
    col_block = jnp.arange(owned_cols, dtype=jnp.int32) // BLK
    own_col = col_block[:, None] == slot_block[None, :]

    def own_half(full_t):
        parts = full_t.reshape(owned_blocks, BLK, slot_count)
        sel = jnp.arange(owned_blocks, dtype=jnp.int32)[:, None, None] == slot_block[None, None, :]
        return jnp.sum(jnp.where(sel, parts, 0.0), axis=0)

    def widen(narrow_t):
        tiled = jnp.tile(narrow_t, (owned_blocks, 1))
        return jnp.where(own_col, tiled, jnp.zeros_like(tiled))

    partial_t = lax.dot_general(
        encoder_weight, got_rows, (((0,), (1,)), ((), ())), preferred_element_type=jnp.float32
    )
    partial = pick_rows(own_half(partial_t), offs_t)
    summed = butterfly_sum(partial, "row")
    bias_t = own_half(jnp.broadcast_to(encoder_bias[:, None], (owned_cols, slot_count)))
    pre_picked = summed + pick_rows(bias_t, offs_t)
    latent_t = spread_rows(pre_picked, offs_t).astype(jnp.bfloat16)
    latent_wide_t = widen(latent_t)
    decoded = lax.dot_general(
        latent_wide_t, decoder_weight, (((0,), (0,)), ((), ())), preferred_element_type=jnp.float32
    ).astype(jnp.bfloat16)
    returned = lax.all_to_all(
        decoded.reshape(owners, per_owner, feature_width),
        "lat",
        split_axis=0,
        concat_axis=0,
        tiled=True,
    ).reshape(slot_count, feature_width)
    rebuilt = lax.dot_general(
        row_hot, returned, (((0,), (0,)), ((), ())), preferred_element_type=jnp.float32
    )
    recon_error = (center_bias[None, :] + rebuilt) - activations
    loss_part = jnp.sum(recon_error * recon_error, axis=1)
    error_b = recon_error.astype(jnp.bfloat16)
    out_error = jnp.dot(row_hot, error_b, preferred_element_type=jnp.float32).astype(jnp.bfloat16)
    got_error = lax.all_to_all(
        out_error.reshape(owners, per_owner, feature_width),
        "lat",
        split_axis=0,
        concat_axis=0,
        tiled=True,
    ).reshape(slot_count, feature_width)
    decoder_grad = lax.dot_general(
        latent_wide_t, got_error, (((1,), (0,)), ((), ())), preferred_element_type=jnp.float32
    ).astype(jnp.bfloat16)
    dlatent_t = lax.dot_general(
        decoder_weight, got_error, (((1,), (1,)), ((), ())), preferred_element_type=jnp.float32
    )
    dlatent_part = pick_rows(own_half(dlatent_t), offs_t)
    loss_row = jnp.zeros((1, slot_count), jnp.float32).at[0, :group_rows].set(loss_part)
    reduced = butterfly_sum(jnp.concatenate([dlatent_part, loss_row], axis=0), "row")
    dlatent = reduced[:PER]
    loss_total = reduced[PER, :group_rows]
    grad_t = spread_rows(dlatent, offs_t).astype(jnp.bfloat16)
    grad_wide_t = widen(grad_t)
    encoder_grad = lax.dot_general(
        got_rows, grad_wide_t, (((0,), (1,)), ((), ())), preferred_element_type=jnp.float32
    ).astype(jnp.bfloat16)
    bias_grad = jnp.sum(grad_wide_t.astype(jnp.float32), axis=1)
    row_loss = loss_total / D
    return (encoder_grad, decoder_grad, bias_grad, row_loss)


def solution(mesh):
    return jax.shard_map(
        per_device,
        mesh=mesh,
        in_specs=(
            P("lat", "row"),
            P("row"),
            P("row", "lat"),
            P("lat"),
            P("lat", "row"),
            P("lat", None),
            P("lat", None, None),
        ),
        out_specs=(P("row", "lat"), P("lat", "row"), P("lat"), P("lat")),
        check_vma=False,
    )
```

```python
import jax
import jax.numpy as jnp
from jax import lax
from jax.sharding import PartitionSpec as P


D = 8192
BLK = 128
KB = 4
PER = 8


def slot_targets(row_blocks, total_blocks, capacity):
    pair_blocks = row_blocks.reshape(-1)
    onehot = (pair_blocks[:, None] == jnp.arange(total_blocks, dtype=jnp.int32)[None, :]).astype(
        jnp.int32
    )
    before = jnp.cumsum(onehot, axis=0) - onehot
    ranking = jnp.sum(before * onehot, axis=1)
    return pair_blocks * capacity + ranking


def pick_rows(values_t, offsets_t):
    lanes = jnp.arange(BLK, dtype=jnp.int32)
    hit = offsets_t[:, None, :] == lanes[None, :, None]
    return jnp.sum(jnp.where(hit, values_t[None, :, :], 0.0), axis=1)


def spread_rows(picked_t, offsets_t):
    lanes = jnp.arange(BLK, dtype=jnp.int32)[:, None]
    out = jnp.zeros((BLK, picked_t.shape[1]), picked_t.dtype)
    for j in range(PER):
        out = jnp.where(offsets_t[j : j + 1, :] == lanes, picked_t[j : j + 1, :], out)
    return out


def butterfly_sum(x, axis):
    size = lax.axis_size(axis)
    step = 1
    while step < size:
        other = lax.ppermute(x, axis, perm=[(i, i ^ step) for i in range(size)])
        x = x + other
        step *= 2
    return x


def device_step(
    activations, center_bias, encoder_weight, encoder_bias, decoder_weight, row_blocks, pick_offsets
):
    group_rows, feature_width = activations.shape
    owners = lax.axis_size("lat")
    owned_blocks = encoder_bias.shape[0] // BLK
    owned_cols = owned_blocks * BLK
    total_blocks = owned_blocks * owners
    capacity = 2 * group_rows * KB // total_blocks
    slot_count = total_blocks * capacity
    per_owner = owned_blocks * capacity
    target = slot_targets(row_blocks, total_blocks, capacity)
    slots = jnp.arange(slot_count, dtype=jnp.int32)

    pair_hot = target[None, :] == slots[:, None]
    row_hot = jnp.any(pair_hot.reshape(slot_count, group_rows, KB), axis=2).astype(jnp.bfloat16)
    pair_hot = pair_hot.astype(jnp.bfloat16)

    centered = (activations - center_bias[None, :]).astype(jnp.bfloat16)
    outgoing = jnp.dot(row_hot, centered, preferred_element_type=jnp.float32).astype(jnp.bfloat16)
    offs_plus = (pick_offsets.reshape(-1, PER) + 1).astype(jnp.bfloat16)
    out_offs_t = lax.dot_general(
        offs_plus, pair_hot, (((0,), (1,)), ((), ())), preferred_element_type=jnp.float32
    ).astype(jnp.int32)
    out_offs = out_offs_t.reshape(PER, owners, per_owner).transpose(1, 0, 2)

    got_offs = lax.all_to_all(out_offs, "lat", split_axis=0, concat_axis=0, tiled=True)
    got_rows = lax.all_to_all(
        outgoing.reshape(owners, per_owner, feature_width),
        "lat",
        split_axis=0,
        concat_axis=0,
        tiled=True,
    )
    got_rows = got_rows.reshape(slot_count, feature_width)
    offs_t = got_offs.transpose(1, 0, 2).reshape(PER, slot_count) - 1

    slot_block = (slots // capacity) % owned_blocks
    col_block = jnp.arange(owned_cols, dtype=jnp.int32) // BLK
    own_col = col_block[:, None] == slot_block[None, :]

    def own_half(full_t):
        parts = full_t.reshape(owned_blocks, BLK, slot_count)
        sel = jnp.arange(owned_blocks, dtype=jnp.int32)[:, None, None] == slot_block[None, None, :]
        return jnp.sum(jnp.where(sel, parts, 0.0), axis=0)

    def widen(narrow_t):
        tiled = jnp.tile(narrow_t, (owned_blocks, 1))
        return jnp.where(own_col, tiled, jnp.zeros_like(tiled))

    partial_t = lax.dot_general(
        encoder_weight, got_rows, (((0,), (1,)), ((), ())), preferred_element_type=jnp.float32
    )
    partial = pick_rows(own_half(partial_t), offs_t)
    summed = butterfly_sum(partial, "row")
    bias_t = own_half(jnp.broadcast_to(encoder_bias[:, None], (owned_cols, slot_count)))
    pre_picked = summed + pick_rows(bias_t, offs_t)
    latent_t = spread_rows(pre_picked, offs_t).astype(jnp.bfloat16)
    latent_wide_t = lax.optimization_barrier(widen(latent_t))
    decoded = lax.dot_general(
        latent_wide_t, decoder_weight, (((0,), (0,)), ((), ())), preferred_element_type=jnp.float32
    ).astype(jnp.bfloat16)
    returned = lax.all_to_all(
        decoded.reshape(owners, per_owner, feature_width),
        "lat",
        split_axis=0,
        concat_axis=0,
        tiled=True,
    ).reshape(slot_count, feature_width)
    rebuilt = lax.dot_general(
        row_hot, returned, (((0,), (0,)), ((), ())), preferred_element_type=jnp.float32
    )
    recon_error = (center_bias[None, :] + rebuilt) - activations
    loss_part = jnp.sum(recon_error * recon_error, axis=1)
    error_b = recon_error.astype(jnp.bfloat16)
    out_error = jnp.dot(row_hot, error_b, preferred_element_type=jnp.float32).astype(jnp.bfloat16)
    got_error = lax.all_to_all(
        out_error.reshape(owners, per_owner, feature_width),
        "lat",
        split_axis=0,
        concat_axis=0,
        tiled=True,
    ).reshape(slot_count, feature_width)
    decoder_grad = lax.dot_general(
        latent_wide_t, got_error, (((1,), (0,)), ((), ())), preferred_element_type=jnp.float32
    ).astype(jnp.bfloat16)
    dlatent_t = lax.dot_general(
        decoder_weight, got_error, (((1,), (1,)), ((), ())), preferred_element_type=jnp.float32
    )
    dlatent_part = pick_rows(own_half(dlatent_t), offs_t)
    loss_row = jnp.zeros((1, slot_count), jnp.float32).at[0, :group_rows].set(loss_part)
    reduced = butterfly_sum(jnp.concatenate([dlatent_part, loss_row], axis=0), "row")
    dlatent = reduced[:PER]
    loss_total = reduced[PER, :group_rows]
    grad_t = spread_rows(dlatent, offs_t).astype(jnp.bfloat16)
    grad_wide_t = widen(grad_t)
    encoder_grad = lax.dot_general(
        got_rows, grad_wide_t, (((0,), (1,)), ((), ())), preferred_element_type=jnp.float32
    ).astype(jnp.bfloat16)
    bias_grad = jnp.sum(grad_wide_t.astype(jnp.float32), axis=1)
    row_loss = loss_total / D
    return (encoder_grad, decoder_grad, bias_grad, row_loss)


def solution(mesh):
    return jax.shard_map(
        device_step,
        mesh=mesh,
        in_specs=(
            P("lat", "row"),
            P("row"),
            P("row", "lat"),
            P("lat"),
            P("lat", "row"),
            P("lat", None),
            P("lat", None, None),
        ),
        out_specs=(P("row", "lat"), P("lat", "row"), P("lat"), P("lat")),
        check_vma=False,
    )
```

```python
import jax
import jax.numpy as jnp
from jax import lax
from jax.sharding import PartitionSpec as P


D = 8192
BLK = 128
KB = 4
PER = 8


def slot_targets(row_blocks, total_blocks, capacity):
    pair_blocks = row_blocks.reshape(-1)
    onehot = (pair_blocks[:, None] == jnp.arange(total_blocks, dtype=jnp.int32)[None, :]).astype(
        jnp.int32
    )
    before = jnp.cumsum(onehot, axis=0) - onehot
    ranking = jnp.sum(before * onehot, axis=1)
    return pair_blocks * capacity + ranking


def pick_rows(values_t, offsets_t):
    lanes = jnp.arange(BLK, dtype=jnp.int32)
    hit = offsets_t[:, None, :] == lanes[None, :, None]
    return jnp.sum(jnp.where(hit, values_t[None, :, :], 0.0), axis=1)


def spread_rows(picked_t, offsets_t):
    lanes = jnp.arange(BLK, dtype=jnp.int32)[:, None]
    out = jnp.zeros((BLK, picked_t.shape[1]), picked_t.dtype)
    for j in range(PER):
        out = jnp.where(offsets_t[j : j + 1, :] == lanes, picked_t[j : j + 1, :], out)
    return out


def butterfly_sum(x, axis):
    size = lax.axis_size(axis)
    step = 1
    while step < size:
        other = lax.ppermute(x, axis, perm=[(i, i ^ step) for i in range(size)])
        x = x + other
        step *= 2
    return x


def device_step(
    activations, center_bias, encoder_weight, encoder_bias, decoder_weight, row_blocks, pick_offsets
):
    group_rows, feature_width = activations.shape
    owners = lax.axis_size("lat")
    owned_blocks = encoder_bias.shape[0] // BLK
    owned_cols = owned_blocks * BLK
    total_blocks = owned_blocks * owners
    capacity = 2 * group_rows * KB // total_blocks
    slot_count = total_blocks * capacity
    per_owner = owned_blocks * capacity
    target = slot_targets(row_blocks, total_blocks, capacity)
    slots = jnp.arange(slot_count, dtype=jnp.int32)

    pair_hot = target[None, :] == slots[:, None]
    row_hot = jnp.any(pair_hot.reshape(slot_count, group_rows, KB), axis=2).astype(jnp.bfloat16)
    pair_hot = pair_hot.astype(jnp.bfloat16)

    centered = (activations - center_bias[None, :]).astype(jnp.bfloat16)
    outgoing = jnp.dot(row_hot, centered, preferred_element_type=jnp.float32).astype(jnp.bfloat16)
    offs_plus = (pick_offsets.reshape(-1, PER) + 1).astype(jnp.bfloat16)
    out_offs_t = lax.dot_general(
        offs_plus, pair_hot, (((0,), (1,)), ((), ())), preferred_element_type=jnp.float32
    ).astype(jnp.int32)
    out_offs = out_offs_t.reshape(PER, owners, per_owner).transpose(1, 0, 2)

    got_offs = lax.all_to_all(out_offs, "lat", split_axis=0, concat_axis=0, tiled=True)
    got_rows = lax.all_to_all(
        outgoing.reshape(owners, per_owner, feature_width),
        "lat",
        split_axis=0,
        concat_axis=0,
        tiled=True,
    )
    got_rows = got_rows.reshape(slot_count, feature_width)
    offs_t = got_offs.transpose(1, 0, 2).reshape(PER, slot_count) - 1

    slot_block = (slots // capacity) % owned_blocks
    col_block = jnp.arange(owned_cols, dtype=jnp.int32) // BLK
    own_col = col_block[:, None] == slot_block[None, :]

    def own_half(full_t):
        parts = full_t.reshape(owned_blocks, BLK, slot_count)
        sel = jnp.arange(owned_blocks, dtype=jnp.int32)[:, None, None] == slot_block[None, None, :]
        return jnp.sum(jnp.where(sel, parts, 0.0), axis=0)

    def widen(narrow_t):
        tiled = jnp.tile(narrow_t, (owned_blocks, 1))
        return jnp.where(own_col, tiled, jnp.zeros_like(tiled))

    partial_t = lax.dot_general(
        encoder_weight, got_rows, (((0,), (1,)), ((), ())), preferred_element_type=jnp.float32
    )
    partial = pick_rows(own_half(partial_t), offs_t)
    summed = butterfly_sum(partial, "row")
    bias_t = own_half(jnp.broadcast_to(encoder_bias[:, None], (owned_cols, slot_count)))
    pre_picked = summed + pick_rows(bias_t, offs_t)
    latent_t = spread_rows(pre_picked, offs_t).astype(jnp.bfloat16)
    latent_wide_t = lax.optimization_barrier(widen(latent_t))
    decoded = lax.dot_general(
        latent_wide_t, decoder_weight, (((0,), (0,)), ((), ())), preferred_element_type=jnp.float32
    ).astype(jnp.bfloat16)
    returned = lax.all_to_all(
        decoded.reshape(owners, per_owner, feature_width),
        "lat",
        split_axis=0,
        concat_axis=0,
        tiled=True,
    ).reshape(slot_count, feature_width)
    rebuilt = lax.dot_general(
        row_hot, returned, (((0,), (0,)), ((), ())), preferred_element_type=jnp.float32
    )
    recon_error = (center_bias[None, :] + rebuilt) - activations
    loss_part = jnp.sum(recon_error * recon_error, axis=1)
    error_b = recon_error.astype(jnp.bfloat16)
    out_error = jnp.dot(row_hot, error_b, preferred_element_type=jnp.float32).astype(jnp.bfloat16)
    got_error = lax.all_to_all(
        out_error.reshape(owners, per_owner, feature_width),
        "lat",
        split_axis=0,
        concat_axis=0,
        tiled=True,
    ).reshape(slot_count, feature_width)
    halves = []
    half = feature_width // 2
    for lo in (0, half):
        halves.append(
            lax.dot_general(
                latent_wide_t,
                got_error[:, lo : lo + half],
                (((1,), (0,)), ((), ())),
                preferred_element_type=jnp.float32,
            ).astype(jnp.bfloat16)
        )
    decoder_grad = jnp.concatenate(halves, axis=1)
    dlatent_t = lax.dot_general(
        decoder_weight, got_error, (((1,), (1,)), ((), ())), preferred_element_type=jnp.float32
    )
    dlatent_part = pick_rows(own_half(dlatent_t), offs_t)
    loss_row = jnp.zeros((1, slot_count), jnp.float32).at[0, :group_rows].set(loss_part)
    reduced = butterfly_sum(jnp.concatenate([dlatent_part, loss_row], axis=0), "row")
    dlatent = reduced[:PER]
    loss_total = reduced[PER, :group_rows]
    grad_t = spread_rows(dlatent, offs_t).astype(jnp.bfloat16)
    grad_wide_t = widen(grad_t)
    encoder_grad = lax.dot_general(
        got_rows, grad_wide_t, (((0,), (1,)), ((), ())), preferred_element_type=jnp.float32
    ).astype(jnp.bfloat16)
    bias_grad = jnp.sum(grad_wide_t.astype(jnp.float32), axis=1)
    row_loss = loss_total / D
    return (encoder_grad, decoder_grad, bias_grad, row_loss)


def solution(mesh):
    return jax.shard_map(
        device_step,
        mesh=mesh,
        in_specs=(
            P("lat", "row"),
            P("row"),
            P("row", "lat"),
            P("lat"),
            P("lat", "row"),
            P("lat", None),
            P("lat", None, None),
        ),
        out_specs=(P("row", "lat"), P("lat", "row"), P("lat"), P("lat")),
        check_vma=False,
    )
```
